512 devices in a mesh: gx: 4 (over x), gy: 8 (over z), gz: 16 (over y, core).
Axes of the slice: x: 4, y: 8, z: 8, core: 2. Of those that a mesh axis runs over, the one named last changes fastest.
Arguments:
- tensor: float32 [16, 512, 8, 4, 1024], P(None, 'gz', 'gy', 'gx'), may hold values from -6 to 6
- factor_var: float32 [16, 8], replicated, may hold values from -1.5 to 1.5
- factor_z: float32 [512, 64], P('gz'), may hold values from -0.25 to 0.25
- factor_y: float32 [256, 64], P('gy'), may hold values from -0.375 to 0.375
- basis: float32 [128, 64], replicated, may hold values from -0.5 to 0.5
Outputs:
- new_basis: float32 [128, 64], P('gx')
The draws below stay inside these ranges and needn't reach their ends.
All inputs are finite; a program needn't handle non-finite values.
Results may differ from the reference program's by a relative error of at most 0.0003.
Values sent between devices are 32-bit elements; how exact they have to be, the bound alone decides.
No kernel may reach another device: no remote copies, remote signals or barrier semaphores. Data moves between devices by JAX's collectives and lax.ppermute only.
A program may use at most 64 MiB of HBM per device.

```python
import math
import jax
import jax.numpy as jnp
from jax import lax

NV = 16
R1 = 64
R2 = 64
R3 = 64
R4 = 8
CX = 32
CY = 32
I1 = 128
I2 = 256
I3 = 512
N_GX = 4
N_GY = 8


def level_of(key, extent, shards, least, top_value):
    level = 1.0
    for dim, shards_of in shards:
        heights = jax.random.uniform(jax.random.fold_in(jax.random.fold_in(key, 6), dim), (shards_of,), jnp.float32, least / len(shards), top_value / len(shards))
        level = level * jnp.repeat(jnp.exp(heights), extent[dim] // shards_of).reshape((-1,) + (1,) * (len(extent) - 1 - dim))
    return level


def centred(own_key, extent, scale, reach, shards=(), dtype=jnp.bfloat16):
    array = jax.random.normal(own_key, extent, jnp.float32) * scale
    if len(shards) > 0:
        array = level_of(own_key, extent, shards, -0.22, 0.18) * array
    return jnp.clip(array, min=-reach, max=reach).astype(dtype)


def setup_inputs(seed: int = 0) -> dict:
    arg_keys = jax.random.split(jax.random.key(seed), 6)
    return {
        "tensor": centred(arg_keys[0], (NV, I3, N_GY, N_GX, CY * CX), 1.0, 6.0, ((1, 16), (2, 8), (3, 4)), jnp.float32),
        "factor_var": centred(arg_keys[1], (NV, R4), NV ** -0.5, 1.5, (), jnp.float32),
        "factor_z": centred(arg_keys[2], (I3, R3), I3 ** -0.5, 0.25, ((0, 16),), jnp.float32),
        "factor_y": centred(arg_keys[3], (I2, R2), I2 ** -0.5, 0.375, ((0, 8),), jnp.float32),
        "basis": centred(arg_keys[4], (I1, R1), I1 ** -0.5, 0.5, (), jnp.float32),
    }


def reference(tensor, factor_var, factor_z, factor_y, basis):
    highest = lax.Precision.HIGHEST
    blocked = tensor.reshape(NV, I3, N_GY, N_GX, CY, CX)
    field = jnp.transpose(blocked, (0, 1, 2, 4, 3, 5)).reshape(NV, I3, I2, I1)
    reduced = jnp.einsum('vr,vzyx->rzyx', factor_var, field, precision=highest)
    core_z = jnp.einsum('zs,rzyx->sryx', factor_z, reduced, precision=highest)
    core_rows = jnp.einsum('yq,sryx->qsrx', factor_y, core_z, precision=highest)
    unfold = core_rows.reshape(-1, core_rows.shape[-1])
    gram = jnp.dot(unfold.T.astype(jnp.float32), unfold.astype(jnp.float32), precision=highest, preferred_element_type=jnp.float32)
    image_full = jnp.dot(gram.astype(jnp.float32), basis.astype(jnp.float32), precision=highest, preferred_element_type=jnp.float32)
    cross_gram = jnp.dot(image_full.T.astype(jnp.float32), image_full.astype(jnp.float32), precision=highest, preferred_element_type=jnp.float32)
    lower = jnp.linalg.cholesky(cross_gram)
    solved = lax.linalg.triangular_solve(lower, image_full, left_side=False, lower=True, transpose_a=True)
    return solved * jnp.float32(math.sqrt(I1))
```

```python
import math

import jax
import jax.numpy as jnp
from jax import lax
from jax.sharding import PartitionSpec as P


def butterfly_sum(value, axis):
    size = lax.axis_size(axis)
    distance = 1
    while distance < size:
        pairs = [(i, i ^ distance) for i in range(size)]
        value = value + lax.ppermute(value, axis, pairs)
        distance *= 2
    return value


def on_device(tensor, factor_var, factor_z, factor_y, basis):
    highest = lax.Precision.HIGHEST
    nvars = tensor.shape[0]
    z_cells = tensor.shape[1]
    y_cells = factor_y.shape[0]
    x_cells = tensor.shape[4] // y_cells
    rank_var = factor_var.shape[1]
    local_field = tensor.reshape(nvars, z_cells, y_cells * x_cells)
    reduced = jnp.einsum("vr,vzm->rzm", factor_var, local_field, precision=highest)
    z_share = factor_z.shape[1] // lax.axis_size("gz")
    core_z = lax.psum_scatter(
        jnp.einsum("zs,rzm->srm", factor_z, reduced, precision=highest),
        "gz",
        scatter_dimension=0,
        tiled=True,
    )
    core_z = core_z.reshape(z_share, rank_var, y_cells, x_cells)
    core_rows = lax.psum_scatter(
        jnp.einsum("yq,sryx->qsrx", factor_y, core_z, precision=highest),
        "gy",
        scatter_dimension=0,
        tiled=True,
    )
    unfold = core_rows.reshape(-1, x_cells)
    offset = lax.axis_index("gx") * x_cells
    gathered = lax.all_gather(unfold, "gx", axis=1, tiled=True)
    gram_rows = jnp.dot(
        unfold.T, gathered, precision=highest, preferred_element_type=jnp.float32
    )
    image_part = jnp.dot(
        gram_rows, basis, precision=highest, preferred_element_type=jnp.float32
    )
    local_image = butterfly_sum(butterfly_sum(image_part, "gz"), "gy")
    cross_part = jnp.dot(
        local_image.T, local_image, precision=highest, preferred_element_type=jnp.float32
    )
    cross_gram = butterfly_sum(cross_part, "gx")
    lower = jnp.linalg.cholesky(cross_gram)
    solved = lax.linalg.triangular_solve(
        lower, local_image, left_side=False, lower=True, transpose_a=True
    )
    scale_factor = jnp.float32(math.sqrt(x_cells * lax.axis_size("gx")))
    return solved * scale_factor


def solution(mesh):
    in_specs = (P(None, "gz", "gy", "gx", None), P(), P("gz", None), P("gy", None), P())
    out_specs = P("gx", None)
    return jax.shard_map(
        on_device, mesh=mesh, in_specs=in_specs, out_specs=out_specs, check_vma=False
    )
```

```python
import math

import jax
import jax.numpy as jnp
from jax import lax
from jax.sharding import PartitionSpec as P


def butterfly_sum(value, axis):
    size = lax.axis_size(axis)
    distance = 1
    while distance < size:
        pairs = [(i, i ^ distance) for i in range(size)]
        value = value + lax.ppermute(value, axis, pairs)
        distance *= 2
    return value


def on_device(tensor, factor_var, factor_z, factor_y, basis):
    highest = lax.Precision.HIGHEST
    nvars = tensor.shape[0]
    z_cells = tensor.shape[1]
    y_cells = factor_y.shape[0]
    x_cells = tensor.shape[4] // y_cells
    rank_var = factor_var.shape[1]
    rank_z = factor_z.shape[1]
    rank_y = factor_y.shape[1]
    n_gz = lax.axis_size("gz")
    n_gy = lax.axis_size("gy")
    halves = n_gz // rank_var
    y_half = y_cells // halves
    me_z = lax.axis_index("gz")
    half = me_z % halves

    field = tensor.reshape(nvars, z_cells, halves, y_half * x_cells)
    reduced = jnp.einsum("vr,vzhm->rhzm", factor_var, field, precision=highest)
    chunks = reduced.reshape(n_gz, z_cells * y_half * x_cells)
    fz_rows = jnp.broadcast_to(factor_z.reshape(1, -1), (n_gz, z_cells * rank_z))
    sent = jnp.concatenate([chunks, fz_rows], axis=1)
    got = lax.all_to_all(sent, "gz", 0, 0, tiled=True)
    all_z = got[:, : z_cells * y_half * x_cells].reshape(n_gz * z_cells, y_half * x_cells)
    fz_all = got[:, z_cells * y_half * x_cells :].reshape(n_gz * z_cells, rank_z)
    core_z = jnp.dot(fz_all.T, all_z, precision=highest, preferred_element_type=jnp.float32)

    s_group = rank_z // n_gy
    core_z = core_z.reshape(n_gy, s_group * y_half * x_cells)
    fy_rows = lax.dynamic_slice_in_dim(factor_y, half * y_half, y_half, 0)
    fy_rows = jnp.broadcast_to(fy_rows.reshape(1, -1), (n_gy, y_half * rank_y))
    sent = jnp.concatenate([core_z, fy_rows], axis=1)
    got = lax.all_to_all(sent, "gy", 0, 0, tiled=True)
    all_y = got[:, : s_group * y_half * x_cells].reshape(n_gy, s_group, y_half, x_cells)
    fy_all = got[:, s_group * y_half * x_cells :].reshape(n_gy, y_half, rank_y)
    partial = jnp.einsum("jyq,jsyx->qsx", fy_all, all_y, precision=highest)

    share = s_group // halves
    keep = lax.dynamic_slice_in_dim(partial, half * share, share, 1)
    send = lax.dynamic_slice_in_dim(partial, (1 - half) * share, share, 1)
    core_rows = keep + lax.ppermute(send, "gz", [(i, i ^ 1) for i in range(n_gz)])

    unfold = core_rows.reshape(-1, x_cells)
    gathered = lax.all_gather(unfold, "gx", axis=1, tiled=True)
    gram_rows = jnp.dot(
        unfold.T, gathered, precision=highest, preferred_element_type=jnp.float32
    )
    image_part = jnp.dot(
        gram_rows, basis, precision=highest, preferred_element_type=jnp.float32
    )
    local_image = butterfly_sum(butterfly_sum(image_part, "gz"), "gy")
    cross_part = jnp.dot(
        local_image.T, local_image, precision=highest, preferred_element_type=jnp.float32
    )
    cross_gram = butterfly_sum(cross_part, "gx")
    lower = jnp.linalg.cholesky(cross_gram)
    solved = lax.linalg.triangular_solve(
        lower, local_image, left_side=False, lower=True, transpose_a=True
    )
    scale_factor = jnp.float32(math.sqrt(x_cells * lax.axis_size("gx")))
    return solved * scale_factor


def solution(mesh):
    in_specs = (P(None, "gz", "gy", "gx", None), P(), P("gz", None), P("gy", None), P())
    out_specs = P("gx", None)
    return jax.shard_map(
        on_device, mesh=mesh, in_specs=in_specs, out_specs=out_specs, check_vma=False
    )
```

```python
import math

import jax
import jax.numpy as jnp
from jax import lax
from jax.sharding import PartitionSpec as P


def butterfly_sum(value, axis):
    size = lax.axis_size(axis)
    distance = 1
    while distance < size:
        pairs = [(i, i ^ distance) for i in range(size)]
        value = value + lax.ppermute(value, axis, pairs)
        distance *= 2
    return value


def on_device(tensor, factor_var, factor_z, factor_y, basis):
    highest = lax.Precision.HIGHEST
    nvars = tensor.shape[0]
    z_cells = tensor.shape[1]
    y_cells = factor_y.shape[0]
    x_cells = tensor.shape[4] // y_cells
    rank_var = factor_var.shape[1]
    rank_z = factor_z.shape[1]
    rank_y = factor_y.shape[1]
    n_gz = lax.axis_size("gz")
    n_gy = lax.axis_size("gy")
    halves = n_gz // rank_var
    y_half = y_cells // halves
    me_z = lax.axis_index("gz")
    half = me_z % halves

    field = tensor.reshape(nvars, z_cells, y_cells * x_cells)
    reduced = jnp.einsum("vr,vzm->rzm", factor_var, field, precision=highest)
    reduced = reduced.reshape(rank_var, z_cells, halves, y_half * x_cells)
    chunks = jnp.transpose(reduced, (0, 2, 1, 3)).reshape(n_gz, -1, 128)
    fz_rows = jnp.broadcast_to(factor_z.reshape(1, -1, 128), (n_gz,) + (z_cells * rank_z // 128, 128))
    sent = jnp.concatenate([chunks, fz_rows], axis=1)
    got = lax.all_to_all(sent, "gz", 0, 0, tiled=True)
    raw_rows = z_cells * y_half * x_cells // 128
    all_z = got[:, :raw_rows].reshape(n_gz * z_cells, y_half * x_cells)
    fz_all = got[:, raw_rows:].reshape(n_gz * z_cells, rank_z)
    core_z = jnp.dot(fz_all.T, all_z, precision=highest, preferred_element_type=jnp.float32)

    s_group = rank_z // n_gy
    core_z = core_z.reshape(n_gy, -1, 128)
    fy_rows = lax.dynamic_slice_in_dim(factor_y, half * y_half, y_half, 0)
    fy_rows = jnp.broadcast_to(fy_rows.reshape(1, -1, 128), (n_gy, y_half * rank_y // 128, 128))
    sent = jnp.concatenate([core_z, fy_rows], axis=1)
    got = lax.all_to_all(sent, "gy", 0, 0, tiled=True)
    raw_rows = s_group * y_half * x_cells // 128
    all_y = got[:, :raw_rows].reshape(n_gy, s_group, y_half, x_cells)
    fy_all = got[:, raw_rows:].reshape(n_gy, y_half, rank_y)
    partial = jnp.einsum("jyq,jsyx->qsx", fy_all, all_y, precision=highest)

    share = s_group // halves
    keep = lax.dynamic_slice_in_dim(partial, half * share, share, 1)
    send = lax.dynamic_slice_in_dim(partial, (1 - half) * share, share, 1)
    core_rows = keep + lax.ppermute(send, "gz", [(i, i ^ 1) for i in range(n_gz)])

    unfold = core_rows.reshape(-1, x_cells)
    gathered = lax.all_gather(unfold, "gx", axis=1, tiled=True)
    gram_part = jnp.dot(
        gathered.T, gathered, precision=highest, preferred_element_type=jnp.float32
    )
    image_part = jnp.dot(
        gram_part, basis, precision=highest, preferred_element_type=jnp.float32
    )
    image_full = butterfly_sum(butterfly_sum(image_part, "gz"), "gy")
    cross_gram = jnp.dot(
        image_full.T, image_full, precision=highest, preferred_element_type=jnp.float32
    )
    local_image = lax.dynamic_slice_in_dim(image_full, lax.axis_index("gx") * x_cells, x_cells, 0)
    lower = jnp.linalg.cholesky(cross_gram)
    solved = lax.linalg.triangular_solve(
        lower, local_image, left_side=False, lower=True, transpose_a=True
    )
    scale_factor = jnp.float32(math.sqrt(x_cells * lax.axis_size("gx")))
    return solved * scale_factor


def solution(mesh):
    in_specs = (P(None, "gz", "gy", "gx", None), P(), P("gz", None), P("gy", None), P())
    out_specs = P("gx", None)
    return jax.shard_map(
        on_device, mesh=mesh, in_specs=in_specs, out_specs=out_specs, check_vma=False
    )
```

```python
import math

import jax
import jax.numpy as jnp
from jax import lax
from jax.sharding import PartitionSpec as P


def butterfly_sum(value, axis):
    size = lax.axis_size(axis)
    distance = 1
    while distance < size:
        pairs = [(i, i ^ distance) for i in range(size)]
        value = value + lax.ppermute(value, axis, pairs)
        distance *= 2
    return value


def on_device(tensor, factor_var, factor_z, factor_y, basis):
    highest = lax.Precision.HIGHEST
    nvars = tensor.shape[0]
    z_cells = tensor.shape[1]
    y_cells = factor_y.shape[0]
    x_cells = tensor.shape[4] // y_cells
    rank_var = factor_var.shape[1]
    rank_z = factor_z.shape[1]
    rank_y = factor_y.shape[1]
    n_gz = lax.axis_size("gz")
    n_gy = lax.axis_size("gy")
    halves = n_gz // rank_var
    y_half = y_cells // halves
    me_z = lax.axis_index("gz")
    half = me_z % halves

    field = tensor.reshape(nvars, z_cells, y_cells * x_cells)
    reduced = jnp.einsum("vr,vzm->rzm", factor_var, field, precision=highest)
    reduced = lax.optimization_barrier(reduced).reshape(rank_var, z_cells, halves, y_half * x_cells)
    chunks = jnp.transpose(reduced, (0, 2, 1, 3)).reshape(n_gz, -1, 128)
    fz_rows = jnp.broadcast_to(factor_z.reshape(1, -1, 128), (n_gz,) + (z_cells * rank_z // 128, 128))
    sent = jnp.concatenate([chunks, fz_rows], axis=1)
    got = lax.all_to_all(sent, "gz", 0, 0, tiled=True)
    raw_rows = z_cells * y_half * x_cells // 128
    all_z = got[:, :raw_rows].reshape(n_gz * z_cells, y_half * x_cells)
    fz_all = got[:, raw_rows:].reshape(n_gz * z_cells, rank_z)
    core_z = jnp.dot(fz_all.T, all_z, precision=highest, preferred_element_type=jnp.float32)

    s_group = rank_z // n_gy
    core_z = core_z.reshape(n_gy, -1, 128)
    fy_rows = lax.dynamic_slice_in_dim(factor_y, half * y_half, y_half, 0)
    fy_rows = jnp.broadcast_to(fy_rows.reshape(1, -1, 128), (n_gy, y_half * rank_y // 128, 128))
    sent = jnp.concatenate([core_z, fy_rows], axis=1)
    got = lax.all_to_all(sent, "gy", 0, 0, tiled=True)
    raw_rows = s_group * y_half * x_cells // 128
    all_y = got[:, :raw_rows].reshape(n_gy, s_group, y_half, x_cells)
    fy_all = got[:, raw_rows:].reshape(n_gy, y_half, rank_y)
    partial = jnp.einsum("jyq,jsyx->qsx", fy_all, all_y, precision=highest)

    share = s_group // halves
    keep = lax.dynamic_slice_in_dim(partial, half * share, share, 1)
    send = lax.dynamic_slice_in_dim(partial, (1 - half) * share, share, 1)
    core_rows = keep + lax.ppermute(send, "gz", [(i, i ^ 1) for i in range(n_gz)])

    unfold = core_rows.reshape(-1, x_cells)
    gathered = lax.all_gather(unfold, "gx", axis=1, tiled=True)
    gram_part = jnp.dot(
        gathered.T, gathered, precision=highest, preferred_element_type=jnp.float32
    )
    image_part = jnp.dot(
        gram_part, basis, precision=highest, preferred_element_type=jnp.float32
    )
    image_full = butterfly_sum(butterfly_sum(image_part, "gz"), "gy")
    cross_gram = jnp.dot(
        image_full.T, image_full, precision=highest, preferred_element_type=jnp.float32
    )
    local_image = lax.dynamic_slice_in_dim(image_full, lax.axis_index("gx") * x_cells, x_cells, 0)
    lower = jnp.linalg.cholesky(cross_gram)
    solved = lax.linalg.triangular_solve(
        lower, local_image, left_side=False, lower=True, transpose_a=True
    )
    scale_factor = jnp.float32(math.sqrt(x_cells * lax.axis_size("gx")))
    return solved * scale_factor


def solution(mesh):
    in_specs = (P(None, "gz", "gy", "gx", None), P(), P("gz", None), P("gy", None), P())
    out_specs = P("gx", None)
    return jax.shard_map(
        on_device, mesh=mesh, in_specs=in_specs, out_specs=out_specs, check_vma=False
    )
```

```python
import functools
import math

import jax
import jax.numpy as jnp
from jax import lax
from jax.experimental import pallas as pl
from jax.experimental.pallas import tpu as pltpu
from jax.sharding import PartitionSpec as P


def chol_solve_kernel(scale, c_ref, y_ref, o_ref, m_ref):
    n = c_ref.shape[0]
    m_ref[:n, :] = c_ref[...]
    m_ref[n:, :] = y_ref[...]
    lane = lax.broadcasted_iota(jnp.int32, (1, n), 1)

    def step(j, carry):
        m = m_ref[...]
        row = m_ref[pl.ds(j, 1), :]
        pick = lane == j
        col = jnp.sum(jnp.where(pick, m, 0.0), axis=1, keepdims=True)
        pivot = jnp.sum(jnp.where(pick, row, 0.0), axis=1, keepdims=True)
        inv = 1.0 / jnp.sqrt(pivot)
        new_col = col * inv
        l_row = jnp.where(lane > j, row * inv, 0.0)
        m_ref[...] = jnp.where(pick, new_col, m - new_col * l_row)
        return carry

    lax.fori_loop(0, n, step, 0)
    o_ref[...] = m_ref[n:, :] * scale


def chol_solve(cross, image, scale):
    n = cross.shape[0]
    rows = image.shape[0]
    return pl.pallas_call(
        functools.partial(chol_solve_kernel, scale),
        out_shape=jax.ShapeDtypeStruct((rows, n), jnp.float32),
        in_specs=[pl.BlockSpec(memory_space=pltpu.VMEM)] * 2,
        out_specs=pl.BlockSpec(memory_space=pltpu.VMEM),
        scratch_shapes=[pltpu.VMEM((n + rows, n), jnp.float32)],
    )(cross, image)


def butterfly_sum(value, axis):
    size = lax.axis_size(axis)
    distance = 1
    while distance < size:
        pairs = [(i, i ^ distance) for i in range(size)]
        value = value + lax.ppermute(value, axis, pairs)
        distance *= 2
    return value


def on_device(tensor, factor_var, factor_z, factor_y, basis):
    highest = lax.Precision.HIGHEST
    nvars = tensor.shape[0]
    z_cells = tensor.shape[1]
    y_cells = factor_y.shape[0]
    x_cells = tensor.shape[4] // y_cells
    rank_var = factor_var.shape[1]
    rank_z = factor_z.shape[1]
    rank_y = factor_y.shape[1]
    n_gz = lax.axis_size("gz")
    n_gy = lax.axis_size("gy")
    halves = n_gz // rank_var
    y_half = y_cells // halves
    me_z = lax.axis_index("gz")
    half = me_z % halves

    field = tensor.reshape(nvars, z_cells, y_cells * x_cells)
    reduced = jnp.einsum("vr,vzm->rzm", factor_var, field, precision=highest)
    reduced = lax.optimization_barrier(reduced).reshape(rank_var, z_cells, halves, y_half * x_cells)
    chunks = jnp.transpose(reduced, (0, 2, 1, 3)).reshape(n_gz, -1, 128)
    fz_rows = jnp.broadcast_to(factor_z.reshape(1, -1, 128), (n_gz,) + (z_cells * rank_z // 128, 128))
    sent = jnp.concatenate([chunks, fz_rows], axis=1)
    got = lax.all_to_all(sent, "gz", 0, 0, tiled=True)
    raw_rows = z_cells * y_half * x_cells // 128
    all_z = got[:, :raw_rows].reshape(n_gz * z_cells, y_half * x_cells)
    fz_all = got[:, raw_rows:].reshape(n_gz * z_cells, rank_z)
    core_z = jnp.dot(fz_all.T, all_z, precision=highest, preferred_element_type=jnp.float32)

    s_group = rank_z // n_gy
    core_z = core_z.reshape(n_gy, -1, 128)
    fy_rows = lax.dynamic_slice_in_dim(factor_y, half * y_half, y_half, 0)
    fy_rows = jnp.broadcast_to(fy_rows.reshape(1, -1, 128), (n_gy, y_half * rank_y // 128, 128))
    sent = jnp.concatenate([core_z, fy_rows], axis=1)
    got = lax.all_to_all(sent, "gy", 0, 0, tiled=True)
    raw_rows = s_group * y_half * x_cells // 128
    all_y = got[:, :raw_rows].reshape(n_gy, s_group, y_half, x_cells)
    fy_all = got[:, raw_rows:].reshape(n_gy, y_half, rank_y)
    partial = jnp.einsum("jyq,jsyx->qsx", fy_all, all_y, precision=highest)

    share = s_group // halves
    keep = lax.dynamic_slice_in_dim(partial, half * share, share, 1)
    send = lax.dynamic_slice_in_dim(partial, (1 - half) * share, share, 1)
    core_rows = keep + lax.ppermute(send, "gz", [(i, i ^ 1) for i in range(n_gz)])

    unfold = core_rows.reshape(-1, x_cells)
    gathered = lax.all_gather(unfold, "gx", axis=1, tiled=True)
    gram_part = jnp.dot(
        gathered.T, gathered, precision=highest, preferred_element_type=jnp.float32
    )
    image_part = jnp.dot(
        gram_part, basis, precision=highest, preferred_element_type=jnp.float32
    )
    image_full = butterfly_sum(butterfly_sum(image_part, "gz"), "gy")
    cross_gram = jnp.dot(
        image_full.T, image_full, precision=highest, preferred_element_type=jnp.float32
    )
    local_image = lax.dynamic_slice_in_dim(image_full, lax.axis_index("gx") * x_cells, x_cells, 0)
    scale = math.sqrt(x_cells * lax.axis_size("gx"))
    return chol_solve(cross_gram, local_image, scale)


def solution(mesh):
    in_specs = (P(None, "gz", "gy", "gx", None), P(), P("gz", None), P("gy", None), P())
    out_specs = P("gx", None)
    return jax.shard_map(
        on_device, mesh=mesh, in_specs=in_specs, out_specs=out_specs, check_vma=False
    )
```

```python
import functools
import math

import jax
import jax.numpy as jnp
from jax import lax
from jax.experimental import pallas as pl
from jax.experimental.pallas import tpu as pltpu
from jax.sharding import PartitionSpec as P


def chol_solve_kernel(scale, c_ref, y_ref, o_ref, m_ref):
    n = c_ref.shape[0]
    m_ref[:n, :] = c_ref[...]
    m_ref[n:, :] = y_ref[...]
    lane = lax.broadcasted_iota(jnp.int32, (1, n), 1)

    def step(j, carry):
        m = m_ref[...]
        row = m_ref[pl.ds(j, 1), :]
        pick = lane == j
        col = jnp.sum(jnp.where(pick, m, 0.0), axis=1, keepdims=True)
        pivot = jnp.sum(jnp.where(pick, row, 0.0), axis=1, keepdims=True)
        inv = 1.0 / jnp.sqrt(pivot)
        new_col = col * inv
        l_row = jnp.where(lane > j, row * inv, 0.0)
        m_ref[...] = jnp.where(pick, new_col, m - new_col * l_row)
        return carry

    lax.fori_loop(0, n, step, 0)
    o_ref[...] = m_ref[n:, :] * scale


def chol_solve(cross, image, scale):
    n = cross.shape[0]
    rows = image.shape[0]
    return pl.pallas_call(
        functools.partial(chol_solve_kernel, scale),
        out_shape=jax.ShapeDtypeStruct((rows, n), jnp.float32),
        in_specs=[pl.BlockSpec(memory_space=pltpu.VMEM)] * 2,
        out_specs=pl.BlockSpec(memory_space=pltpu.VMEM),
        scratch_shapes=[pltpu.VMEM((n + rows, n), jnp.float32)],
    )(cross, image)


def butterfly_sum(value, axis):
    size = lax.axis_size(axis)
    distance = 1
    while distance < size:
        pairs = [(i, i ^ distance) for i in range(size)]
        value = value + lax.ppermute(value, axis, pairs)
        distance *= 2
    return value


def on_device(tensor, factor_var, factor_z, factor_y, basis):
    highest = lax.Precision.HIGHEST
    nvars = tensor.shape[0]
    z_cells = tensor.shape[1]
    y_cells = factor_y.shape[0]
    x_cells = tensor.shape[4] // y_cells
    rank_var = factor_var.shape[1]
    rank_z = factor_z.shape[1]
    rank_y = factor_y.shape[1]
    n_gz = lax.axis_size("gz")
    n_gy = lax.axis_size("gy")
    halves = n_gz // rank_var
    y_half = y_cells // halves
    me_z = lax.axis_index("gz")
    half = me_z % halves

    field = tensor.reshape(nvars, z_cells, y_cells * x_cells)
    reduced = jnp.einsum("vr,vzm->rzm", factor_var, field, precision=highest)
    reduced = lax.optimization_barrier(reduced).reshape(rank_var, z_cells, halves, y_half * x_cells)
    chunks = jnp.transpose(reduced, (0, 2, 1, 3)).reshape(n_gz, -1, 128)
    fz_rows = jnp.broadcast_to(factor_z.reshape(1, -1, 128), (n_gz,) + (z_cells * rank_z // 128, 128))
    sent = jnp.concatenate([chunks, fz_rows], axis=1)
    got = lax.all_to_all(sent, "gz", 0, 0, tiled=True)
    raw_rows = z_cells * y_half * x_cells // 128
    all_z = got[:, :raw_rows].reshape(n_gz * z_cells, y_half * x_cells)
    fz_all = got[:, raw_rows:].reshape(n_gz * z_cells, rank_z)
    core_z = jnp.dot(fz_all.T, all_z, precision=highest, preferred_element_type=jnp.float32)

    n_gx = lax.axis_size("gx")
    s_group = rank_z // n_gy
    core_z = core_z.reshape(1, n_gy, -1, 128)
    fy_rows = lax.dynamic_slice_in_dim(factor_y, half * y_half, y_half, 0)
    fy_rows = jnp.broadcast_to(fy_rows.reshape(1, 1, -1, 128), (1, n_gy, y_half * rank_y // 128, 128))
    sent = jnp.concatenate([core_z, fy_rows], axis=2)
    sent = jnp.broadcast_to(sent, (n_gx,) + sent.shape[1:]).reshape((n_gx * n_gy,) + sent.shape[2:])
    got = lax.all_to_all(sent, ("gx", "gy"), 0, 0, tiled=True)
    got = got.reshape((n_gx, n_gy) + got.shape[1:])
    raw_rows = s_group * y_half * x_cells // 128
    all_y = got[:, :, :raw_rows].reshape(n_gx, n_gy, s_group, y_half, x_cells)
    fy_all = got[0, :, raw_rows:].reshape(n_gy, y_half, rank_y)
    partial = jnp.einsum("jyq,bjsyx->qsbx", fy_all, all_y, precision=highest)
    partial = partial.reshape(rank_y, s_group, n_gx * x_cells)

    share = s_group // halves
    keep = lax.dynamic_slice_in_dim(partial, half * share, share, 1)
    send = lax.dynamic_slice_in_dim(partial, (1 - half) * share, share, 1)
    core_rows = keep + lax.ppermute(send, "gz", [(i, i ^ 1) for i in range(n_gz)])
    gathered = core_rows.reshape(-1, n_gx * x_cells)

    gram_part = jnp.dot(
        gathered.T, gathered, precision=highest, preferred_element_type=jnp.float32
    )
    image_part = jnp.dot(
        gram_part, basis, precision=highest, preferred_element_type=jnp.float32
    )
    image_full = butterfly_sum(butterfly_sum(image_part, "gz"), "gy")
    cross_gram = jnp.dot(
        image_full.T, image_full, precision=highest, preferred_element_type=jnp.float32
    )
    local_image = lax.dynamic_slice_in_dim(image_full, lax.axis_index("gx") * x_cells, x_cells, 0)
    scale = math.sqrt(x_cells * lax.axis_size("gx"))
    return chol_solve(cross_gram, local_image, scale)


def solution(mesh):
    in_specs = (P(None, "gz", "gy", "gx", None), P(), P("gz", None), P("gy", None), P())
    out_specs = P("gx", None)
    return jax.shard_map(
        on_device, mesh=mesh, in_specs=in_specs, out_specs=out_specs, check_vma=False
    )
```

```python
import functools
import math

import jax
import jax.numpy as jnp
from jax import lax
from jax.experimental import pallas as pl
from jax.experimental.pallas import tpu as pltpu
from jax.sharding import PartitionSpec as P


def chol_solve_kernel(scale, c_ref, y_ref, o_ref, m_ref):
    n = c_ref.shape[0]
    m_ref[:n, :] = c_ref[...]
    m_ref[n:, :] = y_ref[...]
    lane = lax.broadcasted_iota(jnp.int32, (1, n), 1)

    def step(j, carry):
        m = m_ref[...]
        row = m_ref[pl.ds(j, 1), :]
        pick = lane == j
        col = jnp.sum(jnp.where(pick, m, 0.0), axis=1, keepdims=True)
        pivot = jnp.sum(jnp.where(pick, row, 0.0), axis=1, keepdims=True)
        inv = 1.0 / jnp.sqrt(pivot)
        new_col = col * inv
        l_row = jnp.where(lane > j, row * inv, 0.0)
        m_ref[...] = jnp.where(pick, new_col, m - new_col * l_row)
        return carry

    lax.fori_loop(0, n, step, 0)
    o_ref[...] = m_ref[n:, :] * scale


def chol_solve(cross, image, scale):
    n = cross.shape[0]
    rows = image.shape[0]
    return pl.pallas_call(
        functools.partial(chol_solve_kernel, scale),
        out_shape=jax.ShapeDtypeStruct((rows, n), jnp.float32),
        in_specs=[pl.BlockSpec(memory_space=pltpu.VMEM)] * 2,
        out_specs=pl.BlockSpec(memory_space=pltpu.VMEM),
        scratch_shapes=[pltpu.VMEM((n + rows, n), jnp.float32)],
    )(cross, image)


def butterfly_sum(value, axis):
    size = lax.axis_size(axis)
    distance = 1
    while distance < size:
        pairs = [(i, i ^ distance) for i in range(size)]
        value = value + lax.ppermute(value, axis, pairs)
        distance *= 2
    return value


def on_device(tensor, factor_var, factor_z, factor_y, basis):
    highest = lax.Precision.HIGHEST
    nvars = tensor.shape[0]
    z_cells = tensor.shape[1]
    y_cells = factor_y.shape[0]
    x_cells = tensor.shape[4] // y_cells
    rank_var = factor_var.shape[1]
    rank_z = factor_z.shape[1]
    rank_y = factor_y.shape[1]
    n_gz = lax.axis_size("gz")
    n_gy = lax.axis_size("gy")
    halves = n_gz // rank_var
    y_half = y_cells // halves
    me_z = lax.axis_index("gz")
    half = me_z % halves

    field = tensor.reshape(nvars, z_cells, y_cells * x_cells)
    reduced = jnp.einsum("vr,vzm->rzm", factor_var, field, precision=highest)
    reduced = lax.optimization_barrier(reduced).reshape(rank_var, z_cells, halves, y_half * x_cells)
    chunks = jnp.transpose(reduced, (0, 2, 1, 3)).reshape(n_gz, -1, 128)
    fz_rows = jnp.broadcast_to(factor_z.reshape(1, -1, 128), (n_gz,) + (z_cells * rank_z // 128, 128))
    sent = jnp.concatenate([chunks, fz_rows], axis=1)
    got = lax.all_to_all(sent, "gz", 0, 0, tiled=True)
    raw_rows = z_cells * y_half * x_cells // 128
    all_z = got[:, :raw_rows].reshape(n_gz * z_cells, y_half * x_cells)
    fz_all = got[:, raw_rows:].reshape(n_gz * z_cells, rank_z)
    core_z = jnp.dot(fz_all.T, all_z, precision=highest, preferred_element_type=jnp.float32)

    s_group = rank_z // n_gy
    core_z = core_z.reshape(n_gy, -1, 128)
    fy_rows = lax.dynamic_slice_in_dim(factor_y, half * y_half, y_half, 0)
    fy_rows = jnp.broadcast_to(fy_rows.reshape(1, -1, 128), (n_gy, y_half * rank_y // 128, 128))
    sent = jnp.concatenate([core_z, fy_rows], axis=1)
    got = lax.all_to_all(sent, "gy", 0, 0, tiled=True)
    raw_rows = s_group * y_half * x_cells // 128
    all_y = got[:, :raw_rows].reshape(n_gy, s_group, y_half, x_cells)
    fy_all = got[:, raw_rows:].reshape(n_gy, y_half, rank_y)
    partial = jnp.einsum("jyq,jsyx->qsx", fy_all, all_y, precision=highest)

    share = s_group // halves
    keep = lax.dynamic_slice_in_dim(partial, half * share, share, 1)
    send = lax.dynamic_slice_in_dim(partial, (1 - half) * share, share, 1)
    core_rows = keep + lax.ppermute(send, "gz", [(i, i ^ 1) for i in range(n_gz)])

    unfold = core_rows.reshape(-1, x_cells)
    gathered = lax.all_gather(unfold, "gx", axis=1, tiled=True)
    gram_part = jnp.dot(
        gathered.T, gathered, precision=highest, preferred_element_type=jnp.float32
    )
    image_part = jnp.dot(
        gram_part, basis, precision=highest, preferred_element_type=jnp.float32
    )
    image_full = butterfly_sum(butterfly_sum(image_part, "gy"), "gz")
    cross_gram = jnp.dot(
        image_full.T, image_full, precision=highest, preferred_element_type=jnp.float32
    )
    local_image = lax.dynamic_slice_in_dim(image_full, lax.axis_index("gx") * x_cells, x_cells, 0)
    scale = math.sqrt(x_cells * lax.axis_size("gx"))
    return chol_solve(cross_gram, local_image, scale)


def solution(mesh):
    in_specs = (P(None, "gz", "gy", "gx", None), P(), P("gz", None), P("gy", None), P())
    out_specs = P("gx", None)
    return jax.shard_map(
        on_device, mesh=mesh, in_specs=in_specs, out_specs=out_specs, check_vma=False
    )
```

```python
import functools
import math

import jax
import jax.numpy as jnp
from jax import lax
from jax.experimental import pallas as pl
from jax.experimental.pallas import tpu as pltpu
from jax.sharding import PartitionSpec as P


def chol_solve_kernel(scale, c_ref, y_ref, o_ref, m_ref):
    n = c_ref.shape[0]
    m_ref[:n, :] = c_ref[...]
    m_ref[n:, :] = y_ref[...]
    lane = lax.broadcasted_iota(jnp.int32, (1, n), 1)

    def step(j, carry):
        m = m_ref[...]
        row = m_ref[pl.ds(j, 1), :]
        pick = lane == j
        col = jnp.sum(jnp.where(pick, m, 0.0), axis=1, keepdims=True)
        pivot = jnp.sum(jnp.where(pick, row, 0.0), axis=1, keepdims=True)
        inv = 1.0 / jnp.sqrt(pivot)
        new_col = col * inv
        l_row = jnp.where(lane > j, row * inv, 0.0)
        m_ref[...] = jnp.where(pick, new_col, m - new_col * l_row)
        return carry

    lax.fori_loop(0, n, step, 0)
    o_ref[...] = m_ref[n:, :] * scale


def chol_solve(cross, image, scale):
    n = cross.shape[0]
    rows = image.shape[0]
    return pl.pallas_call(
        functools.partial(chol_solve_kernel, scale),
        out_shape=jax.ShapeDtypeStruct((rows, n), jnp.float32),
        in_specs=[pl.BlockSpec(memory_space=pltpu.VMEM)] * 2,
        out_specs=pl.BlockSpec(memory_space=pltpu.VMEM),
        scratch_shapes=[pltpu.VMEM((n + rows, n), jnp.float32)],
    )(cross, image)


def butterfly_sum(value, axis):
    size = lax.axis_size(axis)
    distance = 1
    while distance < size:
        pairs = [(i, i ^ distance) for i in range(size)]
        value = value + lax.ppermute(value, axis, pairs)
        distance *= 2
    return value


def all_to_all_sum(value, axes):
    groups = 1
    for axis in axes:
        groups *= lax.axis_size(axis)
    pieces = value.reshape(groups, -1)
    got = lax.all_to_all(pieces, axes, 0, 0, tiled=True)
    mine = jnp.sum(got, axis=0, keepdims=True)
    spread = jnp.broadcast_to(mine, pieces.shape)
    return lax.all_to_all(spread, axes, 0, 0, tiled=True).reshape(value.shape)


def on_device(tensor, factor_var, factor_z, factor_y, basis):
    highest = lax.Precision.HIGHEST
    nvars = tensor.shape[0]
    z_cells = tensor.shape[1]
    y_cells = factor_y.shape[0]
    x_cells = tensor.shape[4] // y_cells
    rank_var = factor_var.shape[1]
    rank_z = factor_z.shape[1]
    rank_y = factor_y.shape[1]
    n_gz = lax.axis_size("gz")
    n_gy = lax.axis_size("gy")
    halves = n_gz // rank_var
    y_half = y_cells // halves
    me_z = lax.axis_index("gz")
    half = me_z % halves

    field = tensor.reshape(nvars, z_cells, y_cells * x_cells)
    reduced = jnp.einsum("vr,vzm->rzm", factor_var, field, precision=highest)
    reduced = lax.optimization_barrier(reduced).reshape(rank_var, z_cells, halves, y_half * x_cells)
    chunks = jnp.transpose(reduced, (0, 2, 1, 3)).reshape(n_gz, -1, 128)
    fz_rows = jnp.broadcast_to(factor_z.reshape(1, -1, 128), (n_gz,) + (z_cells * rank_z // 128, 128))
    sent = jnp.concatenate([chunks, fz_rows], axis=1)
    got = lax.all_to_all(sent, "gz", 0, 0, tiled=True)
    raw_rows = z_cells * y_half * x_cells // 128
    all_z = got[:, :raw_rows].reshape(n_gz * z_cells, y_half * x_cells)
    fz_all = got[:, raw_rows:].reshape(n_gz * z_cells, rank_z)
    core_z = jnp.dot(fz_all.T, all_z, precision=highest, preferred_element_type=jnp.float32)

    s_group = rank_z // n_gy
    core_z = core_z.reshape(n_gy, -1, 128)
    fy_rows = lax.dynamic_slice_in_dim(factor_y, half * y_half, y_half, 0)
    fy_rows = jnp.broadcast_to(fy_rows.reshape(1, -1, 128), (n_gy, y_half * rank_y // 128, 128))
    sent = jnp.concatenate([core_z, fy_rows], axis=1)
    got = lax.all_to_all(sent, "gy", 0, 0, tiled=True)
    raw_rows = s_group * y_half * x_cells // 128
    all_y = got[:, :raw_rows].reshape(n_gy, s_group, y_half, x_cells)
    fy_all = got[:, raw_rows:].reshape(n_gy, y_half, rank_y)
    partial = jnp.einsum("jyq,jsyx->qsx", fy_all, all_y, precision=highest)

    share = s_group // halves
    keep = lax.dynamic_slice_in_dim(partial, half * share, share, 1)
    send = lax.dynamic_slice_in_dim(partial, (1 - half) * share, share, 1)
    core_rows = keep + lax.ppermute(send, "gz", [(i, i ^ 1) for i in range(n_gz)])

    unfold = core_rows.reshape(-1, x_cells)
    gathered = lax.all_gather(unfold, "gx", axis=1, tiled=True)
    gram_part = jnp.dot(
        gathered.T, gathered, precision=highest, preferred_element_type=jnp.float32
    )
    image_part = jnp.dot(
        gram_part, basis, precision=highest, preferred_element_type=jnp.float32
    )
    image_full = all_to_all_sum(image_part, ("gy", "gz"))
    cross_gram = jnp.dot(
        image_full.T, image_full, precision=highest, preferred_element_type=jnp.float32
    )
    local_image = lax.dynamic_slice_in_dim(image_full, lax.axis_index("gx") * x_cells, x_cells, 0)
    scale = math.sqrt(x_cells * lax.axis_size("gx"))
    return chol_solve(cross_gram, local_image, scale)


def solution(mesh):
    in_specs = (P(None, "gz", "gy", "gx", None), P(), P("gz", None), P("gy", None), P())
    out_specs = P("gx", None)
    return jax.shard_map(
        on_device, mesh=mesh, in_specs=in_specs, out_specs=out_specs, check_vma=False
    )
```

```python
import functools
import math

import jax
import jax.numpy as jnp
from jax import lax
from jax.experimental import pallas as pl
from jax.experimental.pallas import tpu as pltpu
from jax.sharding import PartitionSpec as P


def chol_solve_kernel(scale, c_ref, y_ref, o_ref, m_ref):
    n = c_ref.shape[0]
    m_ref[:n, :] = c_ref[...]
    m_ref[n:, :] = y_ref[...]
    lane = lax.broadcasted_iota(jnp.int32, (1, n), 1)

    def step(j, carry):
        m = m_ref[...]
        row = m_ref[pl.ds(j, 1), :]
        pick = lane == j
        col = jnp.sum(jnp.where(pick, m, 0.0), axis=1, keepdims=True)
        pivot = jnp.sum(jnp.where(pick, row, 0.0), axis=1, keepdims=True)
        inv = lax.rsqrt(pivot)
        new_col = col * inv
        l_row = jnp.where(lane > j, row * inv, 0.0)
        m_ref[...] = jnp.where(pick, new_col, m - new_col * l_row)
        return carry

    lax.fori_loop(0, n, step, 0)
    o_ref[...] = m_ref[n:, :] * scale


def chol_solve(cross, image, scale):
    n = cross.shape[0]
    rows = image.shape[0]
    return pl.pallas_call(
        functools.partial(chol_solve_kernel, scale),
        out_shape=jax.ShapeDtypeStruct((rows, n), jnp.float32),
        in_specs=[pl.BlockSpec(memory_space=pltpu.VMEM)] * 2,
        out_specs=pl.BlockSpec(memory_space=pltpu.VMEM),
        scratch_shapes=[pltpu.VMEM((n + rows, n), jnp.float32)],
    )(cross, image)


def butterfly_sum(value, axis):
    size = lax.axis_size(axis)
    distance = 1
    while distance < size:
        pairs = [(i, i ^ distance) for i in range(size)]
        value = value + lax.ppermute(value, axis, pairs)
        distance *= 2
    return value


def all_to_all_sum(value, axes):
    groups = 1
    for axis in axes:
        groups *= lax.axis_size(axis)
    pieces = value.reshape(groups, -1)
    got = lax.all_to_all(pieces, axes, 0, 0, tiled=True)
    mine = jnp.sum(got, axis=0, keepdims=True)
    spread = jnp.broadcast_to(mine, pieces.shape)
    return lax.all_to_all(spread, axes, 0, 0, tiled=True).reshape(value.shape)


def on_device(tensor, factor_var, factor_z, factor_y, basis):
    highest = lax.Precision.HIGHEST
    nvars = tensor.shape[0]
    z_cells = tensor.shape[1]
    y_cells = factor_y.shape[0]
    x_cells = tensor.shape[4] // y_cells
    rank_var = factor_var.shape[1]
    rank_z = factor_z.shape[1]
    rank_y = factor_y.shape[1]
    n_gz = lax.axis_size("gz")
    n_gy = lax.axis_size("gy")
    halves = n_gz // rank_var
    y_half = y_cells // halves
    me_z = lax.axis_index("gz")
    half = me_z % halves

    field = tensor.reshape(nvars, z_cells, y_cells * x_cells)
    reduced = jnp.einsum("vr,vzm->rzm", factor_var, field, precision=highest)
    reduced = lax.optimization_barrier(reduced).reshape(rank_var, z_cells, halves, y_half * x_cells)
    chunks = jnp.transpose(reduced, (0, 2, 1, 3)).reshape(n_gz, -1, 128)
    fz_rows = jnp.broadcast_to(factor_z.reshape(1, -1, 128), (n_gz,) + (z_cells * rank_z // 128, 128))
    sent = jnp.concatenate([chunks, fz_rows], axis=1)
    got = lax.all_to_all(sent, "gz", 0, 0, tiled=True)
    raw_rows = z_cells * y_half * x_cells // 128
    all_z = got[:, :raw_rows].reshape(n_gz * z_cells, y_half * x_cells)
    fz_all = got[:, raw_rows:].reshape(n_gz * z_cells, rank_z)
    core_z = jnp.dot(fz_all.T, all_z, precision=highest, preferred_element_type=jnp.float32)

    s_group = rank_z // n_gy
    core_z = core_z.reshape(n_gy, -1, 128)
    fy_rows = lax.dynamic_slice_in_dim(factor_y, half * y_half, y_half, 0)
    fy_rows = jnp.broadcast_to(fy_rows.reshape(1, -1, 128), (n_gy, y_half * rank_y // 128, 128))
    sent = jnp.concatenate([core_z, fy_rows], axis=1)
    got = lax.all_to_all(sent, "gy", 0, 0, tiled=True)
    raw_rows = s_group * y_half * x_cells // 128
    all_y = got[:, :raw_rows].reshape(n_gy, s_group, y_half, x_cells)
    fy_all = got[:, raw_rows:].reshape(n_gy, y_half, rank_y)
    partial = jnp.einsum("jyq,jsyx->qsx", fy_all, all_y, precision=highest)

    share = s_group // halves
    keep = lax.dynamic_slice_in_dim(partial, half * share, share, 1)
    send = lax.dynamic_slice_in_dim(partial, (1 - half) * share, share, 1)
    core_rows = keep + lax.ppermute(send, "gz", [(i, i ^ 1) for i in range(n_gz)])

    unfold = core_rows.reshape(-1, x_cells)
    n_gx = lax.axis_size("gx")
    copies = jnp.broadcast_to(unfold[None], (n_gx,) + unfold.shape)
    blocks = lax.all_to_all(copies, "gx", 0, 0, tiled=True)
    gathered = jnp.transpose(blocks, (1, 0, 2)).reshape(unfold.shape[0], n_gx * x_cells)
    gram_part = jnp.dot(
        gathered.T, gathered, precision=highest, preferred_element_type=jnp.float32
    )
    image_part = jnp.dot(
        gram_part, basis, precision=highest, preferred_element_type=jnp.float32
    )
    image_full = all_to_all_sum(image_part, ("gy", "gz"))
    cross_gram = jnp.dot(
        image_full.T, image_full, precision=highest, preferred_element_type=jnp.float32
    )
    local_image = lax.dynamic_slice_in_dim(image_full, lax.axis_index("gx") * x_cells, x_cells, 0)
    scale = math.sqrt(x_cells * lax.axis_size("gx"))
    return chol_solve(cross_gram, local_image, scale)


def solution(mesh):
    in_specs = (P(None, "gz", "gy", "gx", None), P(), P("gz", None), P("gy", None), P())
    out_specs = P("gx", None)
    return jax.shard_map(
        on_device, mesh=mesh, in_specs=in_specs, out_specs=out_specs, check_vma=False
    )
```

```python
import functools
import math

import jax
import jax.numpy as jnp
from jax import lax
from jax.experimental import pallas as pl
from jax.experimental.pallas import tpu as pltpu
from jax.sharding import PartitionSpec as P


def chol_solve_kernel(scale, img_ref, o_ref, m_ref):
    n = img_ref.shape[1]
    rows = o_ref.shape[0]
    image = img_ref[...]
    m_ref[:n, :] = lax.dot_general(
        image, image, (((0,), (0,)), ((), ())),
        precision=lax.Precision.HIGHEST, preferred_element_type=jnp.float32,
    )
    start = pl.multiple_of(lax.axis_index("gx") * rows, rows)
    m_ref[n:, :] = img_ref[pl.ds(start, rows), :]
    lane = lax.broadcasted_iota(jnp.int32, (1, n), 1)

    def step(j, carry):
        m = m_ref[...]
        row = m_ref[pl.ds(j, 1), :]
        pick = lane == j
        col = jnp.sum(jnp.where(pick, m, 0.0), axis=1, keepdims=True)
        pivot = jnp.sum(jnp.where(pick, row, 0.0), axis=1, keepdims=True)
        inv = lax.rsqrt(pivot)
        new_col = col * inv
        l_row = jnp.where(lane > j, row * inv, 0.0)
        m_ref[...] = jnp.where(pick, new_col, m - new_col * l_row)
        return carry

    lax.fori_loop(0, n, step, 0)
    o_ref[...] = m_ref[n:, :] * scale


def chol_solve(image, rows, scale):
    n = image.shape[1]
    return pl.pallas_call(
        functools.partial(chol_solve_kernel, scale),
        out_shape=jax.ShapeDtypeStruct((rows, n), jnp.float32),
        in_specs=[pl.BlockSpec(memory_space=pltpu.VMEM)],
        out_specs=pl.BlockSpec(memory_space=pltpu.VMEM),
        scratch_shapes=[pltpu.VMEM((n + rows, n), jnp.float32)],
    )(image)


def all_to_all_sum(value, axes):
    groups = 1
    for axis in axes:
        groups *= lax.axis_size(axis)
    pieces = value.reshape(groups, -1)
    got = lax.all_to_all(pieces, axes, 0, 0, tiled=True)
    mine = jnp.sum(got, axis=0, keepdims=True)
    spread = jnp.broadcast_to(mine, pieces.shape)
    return lax.all_to_all(spread, axes, 0, 0, tiled=True).reshape(value.shape)


def on_device(tensor, factor_var, factor_z, factor_y, basis):
    highest = lax.Precision.HIGHEST
    nvars = tensor.shape[0]
    z_cells = tensor.shape[1]
    y_cells = factor_y.shape[0]
    x_cells = tensor.shape[4] // y_cells
    rank_var = factor_var.shape[1]
    rank_z = factor_z.shape[1]
    rank_y = factor_y.shape[1]
    n_gz = lax.axis_size("gz")
    n_gy = lax.axis_size("gy")
    halves = n_gz // rank_var
    y_half = y_cells // halves
    me_z = lax.axis_index("gz")
    half = me_z % halves

    field = tensor.reshape(nvars, z_cells, y_cells * x_cells)
    reduced = jnp.einsum("vr,vzm->rzm", factor_var, field, precision=highest)
    reduced = lax.optimization_barrier(reduced).reshape(rank_var, z_cells, halves, y_half * x_cells)
    chunks = jnp.transpose(reduced, (0, 2, 1, 3)).reshape(n_gz, -1, 128)
    fz_rows = jnp.broadcast_to(factor_z.reshape(1, -1, 128), (n_gz,) + (z_cells * rank_z // 128, 128))
    sent = jnp.concatenate([chunks, fz_rows], axis=1)
    got = lax.all_to_all(sent, "gz", 0, 0, tiled=True)
    raw_rows = z_cells * y_half * x_cells // 128
    all_z = got[:, :raw_rows].reshape(n_gz * z_cells, y_half * x_cells)
    fz_all = got[:, raw_rows:].reshape(n_gz * z_cells, rank_z)
    core_z = jnp.dot(fz_all.T, all_z, precision=highest, preferred_element_type=jnp.float32)

    s_group = rank_z // n_gy
    core_z = core_z.reshape(n_gy, -1, 128)
    fy_rows = lax.dynamic_slice_in_dim(factor_y, half * y_half, y_half, 0)
    fy_rows = jnp.broadcast_to(fy_rows.reshape(1, -1, 128), (n_gy, y_half * rank_y // 128, 128))
    sent = jnp.concatenate([core_z, fy_rows], axis=1)
    got = lax.all_to_all(sent, "gy", 0, 0, tiled=True)
    raw_rows = s_group * y_half * x_cells // 128
    all_y = got[:, :raw_rows].reshape(n_gy, s_group, y_half, x_cells)
    fy_all = got[:, raw_rows:].reshape(n_gy, y_half, rank_y)
    partial = jnp.einsum("jyq,jsyx->qsx", fy_all, all_y, precision=highest)

    share = s_group // halves
    keep = lax.dynamic_slice_in_dim(partial, half * share, share, 1)
    send = lax.dynamic_slice_in_dim(partial, (1 - half) * share, share, 1)
    core_rows = keep + lax.ppermute(send, "gz", [(i, i ^ 1) for i in range(n_gz)])

    unfold = core_rows.reshape(-1, x_cells)
    n_gx = lax.axis_size("gx")
    copies = jnp.broadcast_to(unfold[None], (n_gx,) + unfold.shape)
    blocks = lax.all_to_all(copies, "gx", 0, 0, tiled=True)
    gathered = jnp.transpose(blocks, (1, 0, 2)).reshape(unfold.shape[0], n_gx * x_cells)
    gram_part = jnp.dot(
        gathered.T, gathered, precision=highest, preferred_element_type=jnp.float32
    )
    image_part = jnp.dot(
        gram_part, basis, precision=highest, preferred_element_type=jnp.float32
    )
    image_full = all_to_all_sum(image_part, ("gy", "gz"))
    scale = math.sqrt(x_cells * lax.axis_size("gx"))
    return chol_solve(image_full, x_cells, scale)


def solution(mesh):
    in_specs = (P(None, "gz", "gy", "gx", None), P(), P("gz", None), P("gy", None), P())
    out_specs = P("gx", None)
    return jax.shard_map(
        on_device, mesh=mesh, in_specs=in_specs, out_specs=out_specs, check_vma=False
    )
```

```python
import functools
import math

import jax
import jax.numpy as jnp
from jax import lax
from jax.experimental import pallas as pl
from jax.experimental.pallas import tpu as pltpu
from jax.sharding import PartitionSpec as P


def chol_solve_kernel(scale, img_ref, o_ref, m_ref):
    n = img_ref.shape[1]
    rows = o_ref.shape[0]
    image = img_ref[...]
    m_ref[:n, :] = lax.dot_general(
        image, image, (((0,), (0,)), ((), ())),
        precision=lax.Precision.HIGHEST, preferred_element_type=jnp.float32,
    )
    start = pl.multiple_of(lax.axis_index("gx") * rows, rows)
    m_ref[n:, :] = img_ref[pl.ds(start, rows), :]
    lane = lax.broadcasted_iota(jnp.int32, (1, n), 1)

    def step(i, carry):
        j = 2 * i
        m = m_ref[...]
        r1 = m_ref[pl.ds(j, 1), :]
        r2 = m_ref[pl.ds(j + 1, 1), :]
        p1 = lane == j
        p2 = lane == j + 1
        c1 = jnp.sum(jnp.where(p1, m, 0.0), axis=1, keepdims=True)
        c2 = jnp.sum(jnp.where(p2, m, 0.0), axis=1, keepdims=True)
        a = jnp.sum(jnp.where(p1, r1, 0.0), axis=1, keepdims=True)
        b = jnp.sum(jnp.where(p1, r2, 0.0), axis=1, keepdims=True)
        c = jnp.sum(jnp.where(p2, r2, 0.0), axis=1, keepdims=True)
        i1 = lax.rsqrt(a)
        l21 = b * i1
        i2 = lax.rsqrt(c - l21 * l21)
        n1 = c1 * i1
        n2 = (c2 - n1 * l21) * i2
        rr1 = r1 * i1
        rr2 = (r2 - rr1 * l21) * i2
        later = lane > j + 1
        u1 = jnp.where(later, rr1, 0.0)
        u2 = jnp.where(later, rr2, 0.0)
        upd = m - n1 * u1 - n2 * u2
        m_ref[...] = jnp.where(p1, n1, jnp.where(p2, n2, upd))
        return carry

    lax.fori_loop(0, n // 2, step, 0)
    o_ref[...] = m_ref[n:, :] * scale


def chol_solve(image, rows, scale):
    n = image.shape[1]
    return pl.pallas_call(
        functools.partial(chol_solve_kernel, scale),
        out_shape=jax.ShapeDtypeStruct((rows, n), jnp.float32),
        in_specs=[pl.BlockSpec(memory_space=pltpu.VMEM)],
        out_specs=pl.BlockSpec(memory_space=pltpu.VMEM),
        scratch_shapes=[pltpu.VMEM((n + rows, n), jnp.float32)],
    )(image)


def all_to_all_sum(value, axes):
    groups = 1
    for axis in axes:
        groups *= lax.axis_size(axis)
    pieces = value.reshape(groups, -1)
    got = lax.all_to_all(pieces, axes, 0, 0, tiled=True)
    mine = jnp.sum(got, axis=0, keepdims=True)
    spread = jnp.broadcast_to(mine, pieces.shape)
    return lax.all_to_all(spread, axes, 0, 0, tiled=True).reshape(value.shape)


def on_device(tensor, factor_var, factor_z, factor_y, basis):
    highest = lax.Precision.HIGHEST
    nvars = tensor.shape[0]
    z_cells = tensor.shape[1]
    y_cells = factor_y.shape[0]
    x_cells = tensor.shape[4] // y_cells
    rank_var = factor_var.shape[1]
    rank_z = factor_z.shape[1]
    rank_y = factor_y.shape[1]
    n_gz = lax.axis_size("gz")
    n_gy = lax.axis_size("gy")
    halves = n_gz // rank_var
    y_half = y_cells // halves
    me_z = lax.axis_index("gz")
    half = me_z % halves

    field = tensor.reshape(nvars, z_cells, y_cells * x_cells)
    reduced = jnp.einsum("vr,vzm->rzm", factor_var, field, precision=highest)
    reduced = lax.optimization_barrier(reduced).reshape(rank_var, z_cells, halves, y_half * x_cells)
    chunks = jnp.transpose(reduced, (0, 2, 1, 3)).reshape(n_gz, -1, 128)
    fz_rows = jnp.broadcast_to(factor_z.reshape(1, -1, 128), (n_gz,) + (z_cells * rank_z // 128, 128))
    sent = jnp.concatenate([chunks, fz_rows], axis=1)
    got = lax.all_to_all(sent, "gz", 0, 0, tiled=True)
    raw_rows = z_cells * y_half * x_cells // 128
    all_z = got[:, :raw_rows].reshape(n_gz * z_cells, y_half * x_cells)
    fz_all = got[:, raw_rows:].reshape(n_gz * z_cells, rank_z)
    core_z = jnp.dot(fz_all.T, all_z, precision=highest, preferred_element_type=jnp.float32)

    s_group = rank_z // n_gy
    core_z = core_z.reshape(n_gy, -1, 128)
    fy_rows = lax.dynamic_slice_in_dim(factor_y, half * y_half, y_half, 0)
    fy_rows = jnp.broadcast_to(fy_rows.reshape(1, -1, 128), (n_gy, y_half * rank_y // 128, 128))
    sent = jnp.concatenate([core_z, fy_rows], axis=1)
    got = lax.all_to_all(sent, "gy", 0, 0, tiled=True)
    raw_rows = s_group * y_half * x_cells // 128
    all_y = got[:, :raw_rows].reshape(n_gy, s_group, y_half, x_cells)
    fy_all = got[:, raw_rows:].reshape(n_gy, y_half, rank_y)
    partial = jnp.einsum("jyq,jsyx->qsx", fy_all, all_y, precision=highest)

    share = s_group // halves
    keep = lax.dynamic_slice_in_dim(partial, half * share, share, 1)
    send = lax.dynamic_slice_in_dim(partial, (1 - half) * share, share, 1)
    core_rows = keep + lax.ppermute(send, "gz", [(i, i ^ 1) for i in range(n_gz)])

    unfold = core_rows.reshape(-1, x_cells)
    n_gx = lax.axis_size("gx")
    copies = jnp.broadcast_to(unfold[None], (n_gx,) + unfold.shape)
    blocks = lax.all_to_all(copies, "gx", 0, 0, tiled=True)
    gathered = jnp.transpose(blocks, (1, 0, 2)).reshape(unfold.shape[0], n_gx * x_cells)
    gram_part = jnp.dot(
        gathered.T, gathered, precision=highest, preferred_element_type=jnp.float32
    )
    image_part = jnp.dot(
        gram_part, basis, precision=highest, preferred_element_type=jnp.float32
    )
    image_full = all_to_all_sum(image_part, ("gy", "gz"))
    scale = math.sqrt(x_cells * lax.axis_size("gx"))
    return chol_solve(image_full, x_cells, scale)


def solution(mesh):
    in_specs = (P(None, "gz", "gy", "gx", None), P(), P("gz", None), P("gy", None), P())
    out_specs = P("gx", None)
    return jax.shard_map(
        on_device, mesh=mesh, in_specs=in_specs, out_specs=out_specs, check_vma=False
    )
```

```python
import functools
import math

import jax
import jax.numpy as jnp
from jax import lax
from jax.experimental import pallas as pl
from jax.experimental.pallas import tpu as pltpu
from jax.sharding import PartitionSpec as P


def chol_solve_kernel(scale, img_ref, o_ref, m_ref):
    n = img_ref.shape[1]
    rows = o_ref.shape[0]
    image = img_ref[...]
    m_ref[:n, :] = lax.dot_general(
        image, image, (((0,), (0,)), ((), ())),
        precision=lax.Precision.HIGHEST, preferred_element_type=jnp.float32,
    )
    start = pl.multiple_of(lax.axis_index("gx") * rows, rows)
    m_ref[n:, :] = img_ref[pl.ds(start, rows), :]
    lane = lax.broadcasted_iota(jnp.int32, (1, n), 1)

    width = 4

    def step(i, carry):
        j = width * i
        m = m_ref[...]
        rows = [m_ref[pl.ds(j + a, 1), :] for a in range(width)]
        picks = [lane == j + a for a in range(width)]
        cols = [jnp.sum(jnp.where(p, m, 0.0), axis=1, keepdims=True) for p in picks]
        block = {
            (a, b): jnp.sum(jnp.where(picks[b], rows[a], 0.0), axis=1, keepdims=True)
            for a in range(width)
            for b in range(a + 1)
        }
        low = {}
        new_cols, new_rows = [], []
        for k in range(width):
            pivot = block[(k, k)]
            for t in range(k):
                pivot = pivot - low[(k, t)] * low[(k, t)]
            inv = lax.rsqrt(pivot)
            col, row = cols[k], rows[k]
            for t in range(k):
                col = col - new_cols[t] * low[(k, t)]
                row = row - new_rows[t] * low[(k, t)]
            new_cols.append(col * inv)
            new_rows.append(row * inv)
            for a in range(k + 1, width):
                entry = block[(a, k)]
                for t in range(k):
                    entry = entry - low[(a, t)] * low[(k, t)]
                low[(a, k)] = entry * inv
        later = lane > j + width - 1
        updated = m
        for k in range(width):
            updated = updated - new_cols[k] * jnp.where(later, new_rows[k], 0.0)
        for k in reversed(range(width)):
            updated = jnp.where(picks[k], new_cols[k], updated)
        m_ref[...] = updated
        return carry

    lax.fori_loop(0, n // width, step, 0)
    o_ref[...] = m_ref[n:, :] * scale


def chol_solve(image, rows, scale):
    n = image.shape[1]
    return pl.pallas_call(
        functools.partial(chol_solve_kernel, scale),
        out_shape=jax.ShapeDtypeStruct((rows, n), jnp.float32),
        in_specs=[pl.BlockSpec(memory_space=pltpu.VMEM)],
        out_specs=pl.BlockSpec(memory_space=pltpu.VMEM),
        scratch_shapes=[pltpu.VMEM((n + rows, n), jnp.float32)],
    )(image)


def all_to_all_sum(value, axes):
    groups = 1
    for axis in axes:
        groups *= lax.axis_size(axis)
    pieces = value.reshape(groups, -1)
    got = lax.all_to_all(pieces, axes, 0, 0, tiled=True)
    mine = jnp.sum(got, axis=0, keepdims=True)
    spread = jnp.broadcast_to(mine, pieces.shape)
    return lax.all_to_all(spread, axes, 0, 0, tiled=True).reshape(value.shape)


def on_device(tensor, factor_var, factor_z, factor_y, basis):
    highest = lax.Precision.HIGHEST
    nvars = tensor.shape[0]
    z_cells = tensor.shape[1]
    y_cells = factor_y.shape[0]
    x_cells = tensor.shape[4] // y_cells
    rank_var = factor_var.shape[1]
    rank_z = factor_z.shape[1]
    rank_y = factor_y.shape[1]
    n_gz = lax.axis_size("gz")
    n_gy = lax.axis_size("gy")
    halves = n_gz // rank_var
    y_half = y_cells // halves
    me_z = lax.axis_index("gz")
    half = me_z % halves

    field = tensor.reshape(nvars, z_cells, y_cells * x_cells)
    reduced = jnp.einsum("vr,vzm->rzm", factor_var, field, precision=highest)
    reduced = lax.optimization_barrier(reduced).reshape(rank_var, z_cells, halves, y_half * x_cells)
    chunks = jnp.transpose(reduced, (0, 2, 1, 3)).reshape(n_gz, -1, 128)
    fz_rows = jnp.broadcast_to(factor_z.reshape(1, -1, 128), (n_gz,) + (z_cells * rank_z // 128, 128))
    sent = jnp.concatenate([chunks, fz_rows], axis=1)
    got = lax.all_to_all(sent, "gz", 0, 0, tiled=True)
    raw_rows = z_cells * y_half * x_cells // 128
    all_z = got[:, :raw_rows].reshape(n_gz * z_cells, y_half * x_cells)
    fz_all = got[:, raw_rows:].reshape(n_gz * z_cells, rank_z)
    core_z = jnp.dot(fz_all.T, all_z, precision=highest, preferred_element_type=jnp.float32)

    s_group = rank_z // n_gy
    core_z = core_z.reshape(n_gy, -1, 128)
    fy_rows = lax.dynamic_slice_in_dim(factor_y, half * y_half, y_half, 0)
    fy_rows = jnp.broadcast_to(fy_rows.reshape(1, -1, 128), (n_gy, y_half * rank_y // 128, 128))
    sent = jnp.concatenate([core_z, fy_rows], axis=1)
    got = lax.all_to_all(sent, "gy", 0, 0, tiled=True)
    raw_rows = s_group * y_half * x_cells // 128
    all_y = got[:, :raw_rows].reshape(n_gy, s_group, y_half, x_cells)
    fy_all = got[:, raw_rows:].reshape(n_gy, y_half, rank_y)
    partial = jnp.einsum("jyq,jsyx->qsx", fy_all, all_y, precision=highest)

    share = s_group // halves
    keep = lax.dynamic_slice_in_dim(partial, half * share, share, 1)
    send = lax.dynamic_slice_in_dim(partial, (1 - half) * share, share, 1)
    core_rows = keep + lax.ppermute(send, "gz", [(i, i ^ 1) for i in range(n_gz)])

    unfold = core_rows.reshape(-1, x_cells)
    n_gx = lax.axis_size("gx")
    copies = jnp.broadcast_to(unfold[None], (n_gx,) + unfold.shape)
    blocks = lax.all_to_all(copies, "gx", 0, 0, tiled=True)
    gathered = jnp.transpose(blocks, (1, 0, 2)).reshape(unfold.shape[0], n_gx * x_cells)
    gram_part = jnp.dot(
        gathered.T, gathered, precision=highest, preferred_element_type=jnp.float32
    )
    image_part = jnp.dot(
        gram_part, basis, precision=highest, preferred_element_type=jnp.float32
    )
    image_full = all_to_all_sum(image_part, ("gy", "gz"))
    scale = math.sqrt(x_cells * lax.axis_size("gx"))
    return chol_solve(image_full, x_cells, scale)


def solution(mesh):
    in_specs = (P(None, "gz", "gy", "gx", None), P(), P("gz", None), P("gy", None), P())
    out_specs = P("gx", None)
    return jax.shard_map(
        on_device, mesh=mesh, in_specs=in_specs, out_specs=out_specs, check_vma=False
    )
```

```python
import functools
import math

import jax
import jax.numpy as jnp
from jax import lax
from jax.experimental import pallas as pl
from jax.experimental.pallas import tpu as pltpu
from jax.sharding import PartitionSpec as P


def chol_solve_kernel(scale, img_ref, o_ref, m_ref):
    n = img_ref.shape[1]
    rows = o_ref.shape[0]
    image = img_ref[...]
    m_ref[:n, :] = lax.dot_general(
        image, image, (((0,), (0,)), ((), ())),
        precision=lax.Precision.HIGHEST, preferred_element_type=jnp.float32,
    )
    start = pl.multiple_of(lax.axis_index("gx") * rows, rows)
    m_ref[n:, :] = img_ref[pl.ds(start, rows), :]
    lane = lax.broadcasted_iota(jnp.int32, (1, n), 1)

    width = 4

    def step(i, carry):
        j = width * i
        m = m_ref[...]
        rows = [m_ref[pl.ds(j + a, 1), :] for a in range(width)]
        picks = [lane == j + a for a in range(width)]
        cols = [jnp.sum(jnp.where(p, m, 0.0), axis=1, keepdims=True) for p in picks]
        block = {
            (a, b): jnp.sum(jnp.where(picks[b], rows[a], 0.0), axis=1, keepdims=True)
            for a in range(width)
            for b in range(a + 1)
        }
        low = {}
        new_cols, new_rows = [], []
        for k in range(width):
            pivot = block[(k, k)]
            for t in range(k):
                pivot = pivot - low[(k, t)] * low[(k, t)]
            inv = lax.rsqrt(pivot)
            col, row = cols[k], rows[k]
            for t in range(k):
                col = col - new_cols[t] * low[(k, t)]
                row = row - new_rows[t] * low[(k, t)]
            new_cols.append(col * inv)
            new_rows.append(row * inv)
            for a in range(k + 1, width):
                entry = block[(a, k)]
                for t in range(k):
                    entry = entry - low[(a, t)] * low[(k, t)]
                low[(a, k)] = entry * inv
        later = lane > j + width - 1
        updated = m
        for k in range(width):
            updated = updated - new_cols[k] * jnp.where(later, new_rows[k], 0.0)
        for k in reversed(range(width)):
            updated = jnp.where(picks[k], new_cols[k], updated)
        m_ref[...] = updated
        return carry

    lax.fori_loop(0, n // width, step, 0)
    o_ref[...] = m_ref[n:, :] * scale


def chol_solve(image, rows, scale):
    n = image.shape[1]
    return pl.pallas_call(
        functools.partial(chol_solve_kernel, scale),
        out_shape=jax.ShapeDtypeStruct((rows, n), jnp.float32),
        in_specs=[pl.BlockSpec(memory_space=pltpu.VMEM)],
        out_specs=pl.BlockSpec(memory_space=pltpu.VMEM),
        scratch_shapes=[pltpu.VMEM((n + rows, n), jnp.float32)],
    )(image)


def all_to_all_sum(value, inner, outer):
    n_in = lax.axis_size(inner)
    n_out = lax.axis_size(outer)
    pieces = value.reshape(n_in, -1)
    got = lax.all_to_all(pieces, inner, 0, 0, tiled=True)
    mine = jnp.sum(got, axis=0, keepdims=True)
    spread = jnp.broadcast_to(mine, (n_out * n_in, mine.shape[1]))
    every = lax.all_to_all(spread, (outer, inner), 0, 0, tiled=True)
    return jnp.sum(every.reshape(n_out, n_in, -1), axis=0).reshape(value.shape)


def on_device(tensor, factor_var, factor_z, factor_y, basis):
    highest = lax.Precision.HIGHEST
    nvars = tensor.shape[0]
    z_cells = tensor.shape[1]
    y_cells = factor_y.shape[0]
    x_cells = tensor.shape[4] // y_cells
    rank_var = factor_var.shape[1]
    rank_z = factor_z.shape[1]
    rank_y = factor_y.shape[1]
    n_gz = lax.axis_size("gz")
    n_gy = lax.axis_size("gy")
    halves = n_gz // rank_var
    y_half = y_cells // halves
    me_z = lax.axis_index("gz")
    half = me_z % halves

    field = tensor.reshape(nvars, z_cells, y_cells * x_cells)
    reduced = jnp.einsum("vr,vzm->rzm", factor_var, field, precision=highest)
    reduced = lax.optimization_barrier(reduced).reshape(rank_var, z_cells, halves, y_half * x_cells)
    chunks = jnp.transpose(reduced, (0, 2, 1, 3)).reshape(n_gz, -1, 128)
    fz_rows = jnp.broadcast_to(factor_z.reshape(1, -1, 128), (n_gz,) + (z_cells * rank_z // 128, 128))
    sent = jnp.concatenate([chunks, fz_rows], axis=1)
    got = lax.all_to_all(sent, "gz", 0, 0, tiled=True)
    raw_rows = z_cells * y_half * x_cells // 128
    all_z = got[:, :raw_rows].reshape(n_gz * z_cells, y_half * x_cells)
    fz_all = got[:, raw_rows:].reshape(n_gz * z_cells, rank_z)
    core_z = jnp.dot(fz_all.T, all_z, precision=highest, preferred_element_type=jnp.float32)

    s_group = rank_z // n_gy
    core_z = core_z.reshape(n_gy, -1, 128)
    fy_rows = lax.dynamic_slice_in_dim(factor_y, half * y_half, y_half, 0)
    fy_rows = jnp.broadcast_to(fy_rows.reshape(1, -1, 128), (n_gy, y_half * rank_y // 128, 128))
    sent = jnp.concatenate([core_z, fy_rows], axis=1)
    got = lax.all_to_all(sent, "gy", 0, 0, tiled=True)
    raw_rows = s_group * y_half * x_cells // 128
    all_y = got[:, :raw_rows].reshape(n_gy, s_group, y_half, x_cells)
    fy_all = got[:, raw_rows:].reshape(n_gy, y_half, rank_y)
    partial = jnp.einsum("jyq,jsyx->qsx", fy_all, all_y, precision=highest)

    share = s_group // halves
    keep = lax.dynamic_slice_in_dim(partial, half * share, share, 1)
    send = lax.dynamic_slice_in_dim(partial, (1 - half) * share, share, 1)
    core_rows = keep + lax.ppermute(send, "gz", [(i, i ^ 1) for i in range(n_gz)])

    unfold = core_rows.reshape(-1, x_cells)
    n_gx = lax.axis_size("gx")
    copies = jnp.broadcast_to(unfold[None], (n_gx,) + unfold.shape)
    blocks = lax.all_to_all(copies, "gx", 0, 0, tiled=True)
    gathered = jnp.transpose(blocks, (1, 0, 2)).reshape(unfold.shape[0], n_gx * x_cells)
    gram_part = jnp.dot(
        gathered.T, gathered, precision=highest, preferred_element_type=jnp.float32
    )
    image_part = jnp.dot(
        gram_part, basis, precision=highest, preferred_element_type=jnp.float32
    )
    image_full = all_to_all_sum(image_part, "gz", "gy")
    scale = math.sqrt(x_cells * lax.axis_size("gx"))
    return chol_solve(image_full, x_cells, scale)


def solution(mesh):
    in_specs = (P(None, "gz", "gy", "gx", None), P(), P("gz", None), P("gy", None), P())
    out_specs = P("gx", None)
    return jax.shard_map(
        on_device, mesh=mesh, in_specs=in_specs, out_specs=out_specs, check_vma=False
    )
```

```python
import functools
import math

import jax
import jax.numpy as jnp
from jax import lax
from jax.experimental import pallas as pl
from jax.experimental.pallas import tpu as pltpu
from jax.sharding import PartitionSpec as P


def chol_solve_kernel(scale, img_ref, o_ref, m_ref):
    n = img_ref.shape[1]
    rows = o_ref.shape[0]
    image = img_ref[...]
    m_ref[:n, :] = lax.dot_general(
        image, image, (((0,), (0,)), ((), ())),
        precision=lax.Precision.HIGHEST, preferred_element_type=jnp.float32,
    )
    start = pl.multiple_of(lax.axis_index("gx") * rows, rows)
    m_ref[n:, :] = img_ref[pl.ds(start, rows), :]
    lane = lax.broadcasted_iota(jnp.int32, (1, n), 1)

    width = 4

    def step(i, carry):
        j = width * i
        m = m_ref[...]
        rows = [m_ref[pl.ds(j + a, 1), :] for a in range(width)]
        picks = [lane == j + a for a in range(width)]
        cols = [jnp.sum(jnp.where(p, m, 0.0), axis=1, keepdims=True) for p in picks]
        block = {
            (a, b): jnp.sum(jnp.where(picks[b], rows[a], 0.0), axis=1, keepdims=True)
            for a in range(width)
            for b in range(a + 1)
        }
        low = {}
        new_cols, new_rows = [], []
        for k in range(width):
            pivot = block[(k, k)]
            for t in range(k):
                pivot = pivot - low[(k, t)] * low[(k, t)]
            inv = lax.rsqrt(pivot)
            col, row = cols[k], rows[k]
            for t in range(k):
                col = col - new_cols[t] * low[(k, t)]
                row = row - new_rows[t] * low[(k, t)]
            new_cols.append(col * inv)
            new_rows.append(row * inv)
            for a in range(k + 1, width):
                entry = block[(a, k)]
                for t in range(k):
                    entry = entry - low[(a, t)] * low[(k, t)]
                low[(a, k)] = entry * inv
        later = lane > j + width - 1
        updated = m
        for k in range(width):
            updated = updated - new_cols[k] * jnp.where(later, new_rows[k], 0.0)
        for k in reversed(range(width)):
            updated = jnp.where(picks[k], new_cols[k], updated)
        m_ref[...] = updated
        return carry

    lax.fori_loop(0, n // width, step, 0)
    o_ref[...] = m_ref[n:, :] * scale


def chol_solve(image, rows, scale):
    n = image.shape[1]
    return pl.pallas_call(
        functools.partial(chol_solve_kernel, scale),
        out_shape=jax.ShapeDtypeStruct((rows, n), jnp.float32),
        in_specs=[pl.BlockSpec(memory_space=pltpu.VMEM)],
        out_specs=pl.BlockSpec(memory_space=pltpu.VMEM),
        scratch_shapes=[pltpu.VMEM((n + rows, n), jnp.float32)],
    )(image)


def all_to_all_sum(value, inner, outer):
    n_in = lax.axis_size(inner)
    n_out = lax.axis_size(outer)
    pieces = value.reshape(n_in, -1)
    got = lax.all_to_all(pieces, inner, 0, 0, tiled=True)
    mine = jnp.sum(got, axis=0, keepdims=True)
    spread = jnp.broadcast_to(mine, (n_out * n_in, mine.shape[1]))
    every = lax.all_to_all(spread, (outer, inner), 0, 0, tiled=True)
    return jnp.sum(every.reshape(n_out, n_in, -1), axis=0).reshape(value.shape)


def on_device(tensor, factor_var, factor_z, factor_y, basis):
    highest = lax.Precision.HIGHEST
    nvars = tensor.shape[0]
    z_cells = tensor.shape[1]
    y_cells = factor_y.shape[0]
    x_cells = tensor.shape[4] // y_cells
    rank_var = factor_var.shape[1]
    rank_z = factor_z.shape[1]
    rank_y = factor_y.shape[1]
    n_gz = lax.axis_size("gz")
    n_gy = lax.axis_size("gy")
    halves = n_gz // rank_var
    y_half = y_cells // halves
    me_z = lax.axis_index("gz")
    half = me_z % halves

    field = tensor.reshape(nvars, z_cells, y_cells * x_cells)
    reduced = jnp.einsum("vr,vzm->rzm", factor_var, field, precision=highest)
    reduced = lax.optimization_barrier(reduced).reshape(rank_var, z_cells, halves, y_half * x_cells)
    chunks = jnp.transpose(reduced, (0, 2, 1, 3)).reshape(n_gz, -1, 128)
    fz_rows = jnp.broadcast_to(factor_z.reshape(1, -1, 128), (n_gz,) + (z_cells * rank_z // 128, 128))
    sent = jnp.concatenate([chunks, fz_rows], axis=1)
    got = lax.all_to_all(sent, "gz", 0, 0, tiled=True)
    raw_rows = z_cells * y_half * x_cells // 128
    all_z = got[:, :raw_rows].reshape(n_gz * z_cells, y_half * x_cells)
    fz_all = got[:, raw_rows:].reshape(n_gz * z_cells, rank_z)
    core_z = jnp.dot(fz_all.T, all_z, precision=highest, preferred_element_type=jnp.float32)

    s_group = rank_z // n_gy
    core_z = core_z.reshape(n_gy, -1, 128)
    fy_rows = lax.dynamic_slice_in_dim(factor_y, half * y_half, y_half, 0)
    fy_rows = jnp.broadcast_to(fy_rows.reshape(1, -1, 128), (n_gy, y_half * rank_y // 128, 128))
    sent = jnp.concatenate([core_z, fy_rows], axis=1)
    got = lax.all_to_all(sent, "gy", 0, 0, tiled=True)
    raw_rows = s_group * y_half * x_cells // 128
    all_y = got[:, :raw_rows].reshape(n_gy, s_group, y_half, x_cells)
    fy_all = got[:, raw_rows:].reshape(n_gy, y_half, rank_y)
    partial = jnp.einsum("jyq,jsyx->qsx", fy_all, all_y, precision=highest)

    share = s_group // halves
    keep = lax.dynamic_slice_in_dim(partial, half * share, share, 1)
    send = lax.dynamic_slice_in_dim(partial, (1 - half) * share, share, 1)
    core_rows = keep + lax.ppermute(send, "gz", [(i, i ^ 1) for i in range(n_gz)])

    unfold = core_rows.reshape(-1, x_cells)
    n_gx = lax.axis_size("gx")
    copies = jnp.broadcast_to(unfold[None], (n_gx,) + unfold.shape)
    blocks = lax.all_to_all(copies, "gx", 0, 0, tiled=True)
    gathered = jnp.transpose(blocks, (1, 0, 2)).reshape(unfold.shape[0], n_gx * x_cells)
    gram_part = jnp.dot(
        gathered.T, gathered, precision=highest, preferred_element_type=jnp.float32
    )
    image_part = jnp.dot(
        gram_part, basis, precision=highest, preferred_element_type=jnp.float32
    )
    image_full = all_to_all_sum(image_part, "gy", "gz")
    scale = math.sqrt(x_cells * lax.axis_size("gx"))
    return chol_solve(image_full, x_cells, scale)


def solution(mesh):
    in_specs = (P(None, "gz", "gy", "gx", None), P(), P("gz", None), P("gy", None), P())
    out_specs = P("gx", None)
    return jax.shard_map(
        on_device, mesh=mesh, in_specs=in_specs, out_specs=out_specs, check_vma=False
    )
```

```python
import functools
import math

import jax
import jax.numpy as jnp
from jax import lax
from jax.experimental import pallas as pl
from jax.experimental.pallas import tpu as pltpu
from jax.sharding import PartitionSpec as P


def chol_solve_kernel(scale, img_ref, o_ref, m_ref):
    n = img_ref.shape[1]
    rows = o_ref.shape[0]
    image = img_ref[...]
    m_ref[:n, :] = lax.dot_general(
        image, image, (((0,), (0,)), ((), ())),
        precision=lax.Precision.HIGHEST, preferred_element_type=jnp.float32,
    )
    start = pl.multiple_of(lax.axis_index("gx") * rows, rows)
    m_ref[n:, :] = img_ref[pl.ds(start, rows), :]
    lane = lax.broadcasted_iota(jnp.int32, (1, n), 1)

    width = 4

    def step(i, carry):
        j = width * i
        m = m_ref[...]
        rows = [m_ref[pl.ds(j + a, 1), :] for a in range(width)]
        picks = [lane == j + a for a in range(width)]
        cols = [jnp.sum(jnp.where(p, m, 0.0), axis=1, keepdims=True) for p in picks]
        block = {
            (a, b): jnp.sum(jnp.where(picks[b], rows[a], 0.0), axis=1, keepdims=True)
            for a in range(width)
            for b in range(a + 1)
        }
        low = {}
        new_cols, new_rows = [], []
        for k in range(width):
            pivot = block[(k, k)]
            for t in range(k):
                pivot = pivot - low[(k, t)] * low[(k, t)]
            inv = lax.rsqrt(pivot)
            col, row = cols[k], rows[k]
            for t in range(k):
                col = col - new_cols[t] * low[(k, t)]
                row = row - new_rows[t] * low[(k, t)]
            new_cols.append(col * inv)
            new_rows.append(row * inv)
            for a in range(k + 1, width):
                entry = block[(a, k)]
                for t in range(k):
                    entry = entry - low[(a, t)] * low[(k, t)]
                low[(a, k)] = entry * inv
        later = lane > j + width - 1
        updated = m
        for k in range(width):
            updated = updated - new_cols[k] * jnp.where(later, new_rows[k], 0.0)
        for k in reversed(range(width)):
            updated = jnp.where(picks[k], new_cols[k], updated)
        m_ref[...] = updated
        return carry

    lax.fori_loop(0, n // width, step, 0)
    o_ref[...] = m_ref[n:, :] * scale


def chol_solve(image, rows, scale):
    n = image.shape[1]
    return pl.pallas_call(
        functools.partial(chol_solve_kernel, scale),
        out_shape=jax.ShapeDtypeStruct((rows, n), jnp.float32),
        in_specs=[pl.BlockSpec(memory_space=pltpu.VMEM)],
        out_specs=pl.BlockSpec(memory_space=pltpu.VMEM),
        scratch_shapes=[pltpu.VMEM((n + rows, n), jnp.float32)],
    )(image)


def all_to_all_sum(value, inner, outer):
    n_in = lax.axis_size(inner)
    n_out = lax.axis_size(outer)
    pieces = value.reshape(n_in, -1)
    got = lax.all_to_all(pieces, inner, 0, 0, tiled=True)
    mine = jnp.sum(got, axis=0, keepdims=True)
    across = lax.all_to_all(jnp.broadcast_to(mine, (n_out, mine.shape[1])), outer, 0, 0, tiled=True)
    total = jnp.sum(across, axis=0, keepdims=True)
    every = lax.all_to_all(jnp.broadcast_to(total, pieces.shape), inner, 0, 0, tiled=True)
    return every.reshape(value.shape)


def on_device(tensor, factor_var, factor_z, factor_y, basis):
    highest = lax.Precision.HIGHEST
    nvars = tensor.shape[0]
    z_cells = tensor.shape[1]
    y_cells = factor_y.shape[0]
    x_cells = tensor.shape[4] // y_cells
    rank_var = factor_var.shape[1]
    rank_z = factor_z.shape[1]
    rank_y = factor_y.shape[1]
    n_gz = lax.axis_size("gz")
    n_gy = lax.axis_size("gy")
    halves = n_gz // rank_var
    y_half = y_cells // halves
    me_z = lax.axis_index("gz")
    half = me_z % halves

    field = tensor.reshape(nvars, z_cells, y_cells * x_cells)
    reduced = jnp.einsum("vr,vzm->rzm", factor_var, field, precision=highest)
    reduced = lax.optimization_barrier(reduced).reshape(rank_var, z_cells, halves, y_half * x_cells)
    chunks = jnp.transpose(reduced, (0, 2, 1, 3)).reshape(n_gz, -1, 128)
    fz_rows = jnp.broadcast_to(factor_z.reshape(1, -1, 128), (n_gz,) + (z_cells * rank_z // 128, 128))
    sent = jnp.concatenate([chunks, fz_rows], axis=1)
    got = lax.all_to_all(sent, "gz", 0, 0, tiled=True)
    raw_rows = z_cells * y_half * x_cells // 128
    all_z = got[:, :raw_rows].reshape(n_gz * z_cells, y_half * x_cells)
    fz_all = got[:, raw_rows:].reshape(n_gz * z_cells, rank_z)
    core_z = jnp.dot(fz_all.T, all_z, precision=highest, preferred_element_type=jnp.float32)

    s_group = rank_z // n_gy
    core_z = core_z.reshape(n_gy, -1, 128)
    fy_rows = lax.dynamic_slice_in_dim(factor_y, half * y_half, y_half, 0)
    fy_rows = jnp.broadcast_to(fy_rows.reshape(1, -1, 128), (n_gy, y_half * rank_y // 128, 128))
    sent = jnp.concatenate([core_z, fy_rows], axis=1)
    got = lax.all_to_all(sent, "gy", 0, 0, tiled=True)
    raw_rows = s_group * y_half * x_cells // 128
    all_y = got[:, :raw_rows].reshape(n_gy, s_group, y_half, x_cells)
    fy_all = got[:, raw_rows:].reshape(n_gy, y_half, rank_y)
    partial = jnp.einsum("jyq,jsyx->qsx", fy_all, all_y, precision=highest)

    share = s_group // halves
    keep = lax.dynamic_slice_in_dim(partial, half * share, share, 1)
    send = lax.dynamic_slice_in_dim(partial, (1 - half) * share, share, 1)
    core_rows = keep + lax.ppermute(send, "gz", [(i, i ^ 1) for i in range(n_gz)])

    unfold = core_rows.reshape(-1, x_cells)
    n_gx = lax.axis_size("gx")
    copies = jnp.broadcast_to(unfold[None], (n_gx,) + unfold.shape)
    blocks = lax.all_to_all(copies, "gx", 0, 0, tiled=True)
    gathered = jnp.transpose(blocks, (1, 0, 2)).reshape(unfold.shape[0], n_gx * x_cells)
    gram_part = jnp.dot(
        gathered.T, gathered, precision=highest, preferred_element_type=jnp.float32
    )
    image_part = jnp.dot(
        gram_part, basis, precision=highest, preferred_element_type=jnp.float32
    )
    image_full = all_to_all_sum(image_part, "gz", "gy")
    scale = math.sqrt(x_cells * lax.axis_size("gx"))
    return chol_solve(image_full, x_cells, scale)


def solution(mesh):
    in_specs = (P(None, "gz", "gy", "gx", None), P(), P("gz", None), P("gy", None), P())
    out_specs = P("gx", None)
    return jax.shard_map(
        on_device, mesh=mesh, in_specs=in_specs, out_specs=out_specs, check_vma=False
    )
```

```python
import functools
import math

import jax
import jax.numpy as jnp
from jax import lax
from jax.experimental import pallas as pl
from jax.experimental.pallas import tpu as pltpu
from jax.sharding import PartitionSpec as P


def chol_solve_kernel(scale, img_ref, o_ref, m_ref):
    n = img_ref.shape[1]
    rows = o_ref.shape[0]
    image = img_ref[...]
    m_ref[:n, :] = lax.dot_general(
        image, image, (((0,), (0,)), ((), ())),
        precision=lax.Precision.HIGHEST, preferred_element_type=jnp.float32,
    )
    start = pl.multiple_of(lax.axis_index("gx") * rows, rows)
    m_ref[n:, :] = img_ref[pl.ds(start, rows), :]
    lane = lax.broadcasted_iota(jnp.int32, (1, n), 1)

    width = 4

    def step(i, carry):
        j = width * i
        m = m_ref[...]
        rows = [m_ref[pl.ds(j + a, 1), :] for a in range(width)]
        picks = [lane == j + a for a in range(width)]
        cols = [jnp.sum(jnp.where(p, m, 0.0), axis=1, keepdims=True) for p in picks]
        block = {
            (a, b): jnp.sum(jnp.where(picks[b], rows[a], 0.0), axis=1, keepdims=True)
            for a in range(width)
            for b in range(a + 1)
        }
        low = {}
        new_cols, new_rows = [], []
        for k in range(width):
            pivot = block[(k, k)]
            for t in range(k):
                pivot = pivot - low[(k, t)] * low[(k, t)]
            inv = lax.rsqrt(pivot)
            col, row = cols[k], rows[k]
            for t in range(k):
                col = col - new_cols[t] * low[(k, t)]
                row = row - new_rows[t] * low[(k, t)]
            new_cols.append(col * inv)
            new_rows.append(row * inv)
            for a in range(k + 1, width):
                entry = block[(a, k)]
                for t in range(k):
                    entry = entry - low[(a, t)] * low[(k, t)]
                low[(a, k)] = entry * inv
        later = lane > j + width - 1
        updated = m
        for k in range(width):
            updated = updated - new_cols[k] * jnp.where(later, new_rows[k], 0.0)
        for k in reversed(range(width)):
            updated = jnp.where(picks[k], new_cols[k], updated)
        m_ref[...] = updated
        return carry

    lax.fori_loop(0, n // width, step, 0)
    o_ref[...] = m_ref[n:, :] * scale


def chol_solve(image, rows, scale):
    n = image.shape[1]
    return pl.pallas_call(
        functools.partial(chol_solve_kernel, scale),
        out_shape=jax.ShapeDtypeStruct((rows, n), jnp.float32),
        in_specs=[pl.BlockSpec(memory_space=pltpu.VMEM)],
        out_specs=pl.BlockSpec(memory_space=pltpu.VMEM),
        scratch_shapes=[pltpu.VMEM((n + rows, n), jnp.float32)],
    )(image)


def all_to_all_sum(value, inner, outer):
    n_in = lax.axis_size(inner)
    n_out = lax.axis_size(outer)
    pieces = value.reshape(n_in, -1)
    got = lax.all_to_all(pieces, inner, 0, 0, tiled=True)
    mine = jnp.sum(got, axis=0, keepdims=True)
    spread = jnp.broadcast_to(mine, (n_out * n_in, mine.shape[1]))
    every = lax.all_to_all(spread, (outer, inner), 0, 0, tiled=True)
    return jnp.sum(every.reshape(n_out, n_in, -1), axis=0).reshape(value.shape)


def on_device(tensor, factor_var, factor_z, factor_y, basis):
    highest = lax.Precision.HIGHEST
    nvars = tensor.shape[0]
    z_cells = tensor.shape[1]
    y_cells = factor_y.shape[0]
    x_cells = tensor.shape[4] // y_cells
    rank_var = factor_var.shape[1]
    rank_z = factor_z.shape[1]
    rank_y = factor_y.shape[1]
    n_gz = lax.axis_size("gz")
    n_gy = lax.axis_size("gy")
    halves = n_gz // rank_var
    y_half = y_cells // halves
    me_z = lax.axis_index("gz")
    half = me_z % halves

    field = tensor.reshape(nvars, z_cells, y_cells * x_cells)
    reduced = jnp.einsum("vr,vzm->rzm", factor_var, field, precision=highest)
    reduced = lax.optimization_barrier(reduced).reshape(rank_var, z_cells, halves, y_half * x_cells)
    chunks = jnp.transpose(reduced, (0, 2, 1, 3)).reshape(n_gz, -1, 128)
    fz_rows = jnp.broadcast_to(factor_z.reshape(1, -1, 128), (n_gz,) + (z_cells * rank_z // 128, 128))
    sent = jnp.concatenate([chunks, fz_rows], axis=1)
    got = lax.all_to_all(sent, "gz", 0, 0, tiled=True)
    raw_rows = z_cells * y_half * x_cells // 128
    all_z = got[:, :raw_rows].reshape(n_gz * z_cells, y_half * x_cells)
    fz_all = got[:, raw_rows:].reshape(n_gz * z_cells, rank_z)
    core_z = jnp.dot(fz_all.T, all_z, precision=highest, preferred_element_type=jnp.float32)

    s_group = rank_z // n_gy
    core_z = core_z.reshape(n_gy, -1, 128)
    fy_rows = lax.dynamic_slice_in_dim(factor_y, half * y_half, y_half, 0)
    fy_rows = jnp.broadcast_to(fy_rows.reshape(1, -1, 128), (n_gy, y_half * rank_y // 128, 128))
    sent = jnp.concatenate([core_z, fy_rows], axis=1)
    got = lax.all_to_all(sent, "gy", 0, 0, tiled=True)
    raw_rows = s_group * y_half * x_cells // 128
    all_y = got[:, :raw_rows].reshape(n_gy, s_group, y_half, x_cells)
    fy_all = got[:, raw_rows:].reshape(n_gy, y_half, rank_y)
    partial = jnp.einsum("jyq,jsyx->qsx", fy_all, all_y, precision=highest)

    share = s_group // halves
    keep = lax.dynamic_slice_in_dim(partial, half * share, share, 1)
    send = lax.dynamic_slice_in_dim(partial, (1 - half) * share, share, 1)
    core_rows = keep + lax.ppermute(send, "gz", [(i, i ^ 1) for i in range(n_gz)])

    unfold = core_rows.reshape(-1, x_cells)
    n_gx = lax.axis_size("gx")
    copies = jnp.broadcast_to(unfold[None], (n_gx,) + unfold.shape)
    blocks = lax.all_to_all(copies, "gx", 0, 0, tiled=True)
    gathered = jnp.transpose(blocks, (1, 0, 2)).reshape(unfold.shape[0], n_gx * x_cells)
    projected = jnp.dot(gathered, basis, precision=highest, preferred_element_type=jnp.float32)
    image_part = jnp.dot(
        gathered.T, projected, precision=highest, preferred_element_type=jnp.float32
    )
    image_full = all_to_all_sum(image_part, "gz", "gy")
    scale = math.sqrt(x_cells * lax.axis_size("gx"))
    return chol_solve(image_full, x_cells, scale)


def solution(mesh):
    in_specs = (P(None, "gz", "gy", "gx", None), P(), P("gz", None), P("gy", None), P())
    out_specs = P("gx", None)
    return jax.shard_map(
        on_device, mesh=mesh, in_specs=in_specs, out_specs=out_specs, check_vma=False
    )
```
